512 devices in a mesh: lon: 32 (over y, x), tm: 16 (over z, core).
Axes of the slice: x: 4, y: 8, z: 8, core: 2. Of those that a mesh axis runs over, the one named last changes fastest.
Arguments:
- anomalies: bfloat16 [4096, 8192], P('lon', 'tm'), may hold values from -200 to 200, as said below
- neighbor_ids: int32 [16, 3], replicated, may hold values from 0 to 15, as said below
- neighbor_counts: int32 [16], replicated, may hold values from 1 to 3
- lag_set: int32 [9], replicated, may hold values from 0 to 128, as said below
Outputs:
- network: float32 [4096, 6912], P(('lon', 'tm'))
The draws below stay inside these ranges and needn't reach their ends.
Inputs may be any that keep to these rules, and one draw needn't show every extreme that they name: `neighbor_ids`: row b lists 3 distinct blocks, each within loop distance 2 of block b (b itself may appear); only the first neighbor_counts[b] slots are used. `lag_set`: 9 distinct lags. Real-valued anomalies; no point's series is constant.
All inputs are finite; a program needn't handle non-finite values.
Results may differ from the reference program's by a relative error of at most 0.0037.
Values may be sent and summed in bfloat16 or wider, within the bound.
No kernel may reach another device: no remote copies, remote signals or barrier semaphores. Data moves between devices by JAX's collectives and lax.ppermute only.
A program may use at most 64 MiB of HBM per device.

```python
import math
import jax
import jax.numpy as jnp
from jax import lax

BLOCK = 256
LMAX = 128
NLAG = 9
K_SLOTS = 3
REACH = 2
BLOCKS = 16
POINTS = 4096
DAYS = 8192


def draw_anomalies(key, part):
    key_base, key_scale = jax.random.split(key, 2)
    point_scale = jnp.exp(jax.random.uniform(key_scale, (POINTS, 1), jnp.float32, 0.0, math.log(10.0)))
    day_ramp = 1.0 + 2.0 * jnp.arange(DAYS, dtype=jnp.float32)[None, :] / (DAYS - 1)
    noise = jnp.clip(jax.random.normal(key_base, (POINTS, DAYS), jnp.float32), -6.0, 6.0)
    values = noise * day_ramp * point_scale
    return values.astype(jnp.bfloat16)


def draw_neighbor_ids(key, part):
    width = 2 * REACH + 1
    block_keys = jax.random.split(key, BLOCKS)
    orders = jax.vmap(lambda block_key: jax.random.permutation(block_key, width))(block_keys)
    offsets = orders - REACH
    first_priority = jnp.where(offsets[0] == REACH, -2, jnp.where(offsets[0] == -1, -1, orders[0]))
    first_row = offsets[0][jnp.argsort(first_priority)]
    second_priority = jnp.where(offsets[1] == -1, -1, orders[1])
    second_row = offsets[1][jnp.argsort(second_priority)]
    last_priority = jnp.where(offsets[BLOCKS - 1] == REACH, -2, jnp.where(offsets[BLOCKS - 1] == 1, -1, orders[BLOCKS - 1]))
    last_row = offsets[BLOCKS - 1][jnp.argsort(last_priority)]
    offsets = offsets.at[0].set(first_row).at[1].set(second_row).at[BLOCKS - 1].set(last_row)
    block_base = jnp.arange(BLOCKS, dtype=jnp.int32)[:, None]
    return ((block_base + offsets[:, :K_SLOTS]) % BLOCKS).astype(jnp.int32)


def draw_neighbor_counts(key, part):
    counts = jax.random.randint(key, (BLOCKS,), 1, K_SLOTS + 1, dtype=jnp.int32)
    return counts.at[0].set(K_SLOTS).at[1].set(1).at[BLOCKS - 1].set(K_SLOTS).astype(jnp.int32)


def draw_lag_set(key, part):
    key_pick, key_order = jax.random.split(key)
    middle = jax.random.permutation(key_pick, LMAX - 1)[:NLAG - 2] + 1
    values = jnp.concatenate([jnp.array([0, LMAX], dtype=jnp.int32), middle.astype(jnp.int32)])
    placing = jax.random.permutation(key_order, NLAG)
    return values[placing].astype(jnp.int32)


def setup_inputs(seed: int = 0) -> dict:
    arg_keys = jax.random.split(jax.random.key(seed), 5)
    return {
        "anomalies": draw_anomalies(jax.random.fold_in(arg_keys[4], 71), 0),
        "neighbor_ids": draw_neighbor_ids(jax.random.fold_in(arg_keys[4], 71), 0),
        "neighbor_counts": draw_neighbor_counts(jax.random.fold_in(arg_keys[4], 71), 0),
        "lag_set": draw_lag_set(jax.random.fold_in(arg_keys[4], 71), 0),
    }


def lagged_product(block_rows, columns, lag_days, day_count):
    left_side = jnp.concatenate([block_rows[:, :day_count], lax.dynamic_slice_in_dim(block_rows, lag_days, day_count, 1)], 1)
    right_side = jnp.concatenate([lax.dynamic_slice_in_dim(columns, lag_days, day_count, 1), columns[:, :day_count]], 1)
    return lax.dot_general(left_side, right_side, (((1,), (1,)), ((), ())), preferred_element_type=jnp.float32)

def reference(anomalies, neighbor_ids, neighbor_counts, lag_set):
    values = anomalies.astype(jnp.float32)
    point_mean = lax.optimization_barrier(jnp.mean(values, axis=1, keepdims=True))
    point_m2 = lax.optimization_barrier(jnp.sum(jnp.square(values - point_mean), axis=1, keepdims=True))
    spread = jnp.sqrt(point_m2 / DAYS + 1e-06)
    standardized = ((values - point_mean) / spread).astype(jnp.bfloat16)
    padded = jnp.concatenate([standardized, jnp.zeros((POINTS, LMAX), jnp.bfloat16)], 1)
    denominator = 2.0 * (DAYS - lag_set).astype(jnp.float32)

    def one_block(block_index):
        block_rows = lax.dynamic_slice_in_dim(padded, block_index * BLOCK, BLOCK, 0)
        live_count = neighbor_counts[block_index]
        pieces = []
        for slot_index in range(K_SLOTS):
            target = neighbor_ids[block_index, slot_index]
            columns = lax.dynamic_slice_in_dim(padded, target * BLOCK, BLOCK, 0)
            for lag_index in range(NLAG):
                product = lagged_product(block_rows, columns, lag_set[lag_index], DAYS)
                linked = product / denominator[lag_index]
                pieces.append(jnp.where(slot_index < live_count, linked, jnp.zeros_like(linked)))
        stacked = jnp.stack(pieces, 1)
        squares = lax.optimization_barrier(jnp.sum(jnp.square(stacked), axis=(1, 2)))
        row_scale = jnp.sqrt(squares / (live_count * NLAG * BLOCK).astype(jnp.float32) + 1e-06)
        return (stacked / row_scale[:, None, None]).reshape(BLOCK, K_SLOTS * NLAG * BLOCK)
    network = lax.map(one_block, jnp.arange(BLOCKS, dtype=jnp.int32))
    return network.reshape(POINTS, K_SLOTS * NLAG * BLOCK)
```

```python
import jax
import jax.numpy as jnp
from jax import lax
from jax.sharding import PartitionSpec as P

LMAX = 128
NLAG = 9
K_SLOTS = 3
REACH = 2


def shifted(value, axis, by):
    size = lax.axis_size(axis)
    pairs = [(i, i + by) for i in range(size) if 0 <= i + by < size]
    return lax.ppermute(value, axis, pairs)


def from_partner(value, axis, stride):
    mask = 2**stride
    pairs = [(source, source ^ mask) for source in range(lax.axis_size(axis))]
    return lax.ppermute(value, axis, pairs)


def shifted_2(value, axis, by):
    size = lax.axis_size(axis)
    return lax.ppermute(value, axis, [(i, (i + by) % size) for i in range(size)])


def local(anomalies, neighbor_ids, neighbor_counts, lag_set):
    half_rows, days_dev = anomalies.shape
    tm_size = lax.axis_size("tm")
    blocks = lax.axis_size("lon") // 2
    block_width = 2 * half_rows
    total_days = days_dev * tm_size
    values = anomalies.astype(jnp.float32)
    shard_mean = jnp.mean(values, axis=1)
    shard_square = jnp.sum(jnp.square(values - shard_mean[:, None]), axis=1)
    stats = lax.all_gather(jnp.stack([shard_mean, shard_square], 0), "tm")
    means, squares = stats[:, 0], stats[:, 1]
    point_mean = jnp.mean(means, axis=0)
    point_m2 = jnp.sum(squares, axis=0) + days_dev * jnp.sum(
        jnp.square(means - point_mean[None, :]), axis=0
    )
    spread = jnp.sqrt(point_m2 / total_days + 1e-06)
    standardized = ((values - point_mean[:, None]) / spread[:, None]).astype(jnp.bfloat16)
    margin = shifted(standardized[:, :LMAX], "tm", -1)
    extended = jnp.concatenate([standardized, margin], 1)
    partner = from_partner(extended, "lon", 0)
    lon_index = lax.axis_index("lon")
    parity = lon_index % 2
    own_block = jnp.where(
        parity == 0,
        jnp.concatenate([extended, partner], 0),
        jnp.concatenate([partner, extended], 0),
    )
    block_index = lon_index // 2
    later_blocks = []
    earlier_blocks = []
    for offset in range(1, REACH + 1):
        later_blocks.append(shifted_2(own_block, "lon", -2 * offset))
        earlier_blocks.append(shifted_2(own_block, "lon", 2 * offset))
    candidates = jnp.stack(earlier_blocks[::-1] + [own_block] + later_blocks, 0)
    block_ids = lax.dynamic_index_in_dim(neighbor_ids, block_index, 0, keepdims=False)
    live_count = lax.dynamic_index_in_dim(neighbor_counts, block_index, 0, keepdims=False)
    positions = (block_ids - block_index + REACH) % blocks

    padded = jnp.concatenate(
        [
            jnp.zeros((half_rows, LMAX), jnp.bfloat16),
            extended[:, :days_dev],
            jnp.zeros((half_rows, LMAX), jnp.bfloat16),
        ],
        1,
    )
    left_rows = []
    for lag_index in range(NLAG):
        lag_days = lag_set[lag_index]
        left_rows.append(
            jnp.concatenate(
                [
                    lax.dynamic_slice_in_dim(padded, LMAX - lag_days, days_dev + LMAX, 1),
                    lax.dynamic_slice_in_dim(extended, lag_days, days_dev, 1),
                ],
                1,
            )
        )
    left = jnp.concatenate(left_rows, 0)
    right_rows = []
    for slot_index in range(K_SLOTS):
        columns = lax.dynamic_index_in_dim(candidates, positions[slot_index], 0, keepdims=False)
        right_rows.append(jnp.concatenate([columns, columns[:, :days_dev]], 1))
    right = jnp.concatenate(right_rows, 0)
    product = lax.dot_general(
        left, right, (((1,), (1,)), ((), ())), preferred_element_type=jnp.float32
    )
    product = product.reshape(NLAG, half_rows, K_SLOTS, block_width)
    product = product.transpose(1, 2, 0, 3).reshape(half_rows, -1)

    out_rows = half_rows // tm_size
    comoment = lax.psum_scatter(product, "tm", scatter_dimension=0, tiled=True)
    comoment = comoment.reshape(out_rows, K_SLOTS, NLAG, block_width)
    denominator = 2.0 * (total_days - lag_set).astype(jnp.float32)
    is_live = jnp.arange(K_SLOTS, dtype=jnp.int32) < live_count
    linked = jnp.where(
        is_live[None, :, None, None], comoment / denominator[None, None, :, None], 0.0
    )
    squares = jnp.sum(jnp.square(linked), axis=(1, 2, 3))
    row_scale = jnp.sqrt(squares / (live_count * NLAG * block_width).astype(jnp.float32) + 1e-06)
    return (linked / row_scale[:, None, None, None]).reshape(out_rows, -1)


def solution(mesh):
    return jax.shard_map(
        local,
        mesh=mesh,
        in_specs=(P("lon", "tm"), P(), P(), P()),
        out_specs=P(("lon", "tm"), None),
        check_vma=False,
    )
```

```python
import jax
import jax.numpy as jnp
from jax import lax
from jax.sharding import PartitionSpec as P

LMAX = 128
NLAG = 9
K_SLOTS = 3
REACH = 2


def shifted(value, axis, by):
    size = lax.axis_size(axis)
    pairs = [(i, i + by) for i in range(size) if 0 <= i + by < size]
    return lax.ppermute(value, axis, pairs)


def from_partner(value, axis, stride):
    mask = 2**stride
    pairs = [(source, source ^ mask) for source in range(lax.axis_size(axis))]
    return lax.ppermute(value, axis, pairs)


def shifted_2(value, axis, by):
    size = lax.axis_size(axis)
    return lax.ppermute(value, axis, [(i, (i + by) % size) for i in range(size)])


def local(anomalies, neighbor_ids, neighbor_counts, lag_set):
    half_rows, days_dev = anomalies.shape
    tm_size = lax.axis_size("tm")
    lon_size = lax.axis_size("lon")
    blocks = lon_size // 2
    block_width = 2 * half_rows
    total_days = days_dev * tm_size
    margin = shifted(anomalies[:, :LMAX], "tm", -1)
    extended = jnp.concatenate([anomalies, margin], 1)
    lon_index = lax.axis_index("lon")
    parity = lon_index % 2
    block_index = lon_index // 2
    reach = 2 * REACH + 1
    halves = []
    for offset in range(-reach, reach + 1):
        if offset == 0:
            halves.append(extended)
            continue
        pairs = []
        for target in range(lon_size):
            low = -2 * REACH - target % 2
            if low <= offset <= low + 2 * (2 * REACH + 1) - 1:
                pairs.append(((target + offset) % lon_size, target))
        halves.append(lax.ppermute(extended, "lon", pairs))
    halves = jnp.stack(halves, 0)
    block_ids = lax.dynamic_index_in_dim(neighbor_ids, block_index, 0, keepdims=False)
    live_count = lax.dynamic_index_in_dim(neighbor_counts, block_index, 0, keepdims=False)
    positions = (block_ids - block_index + REACH) % blocks
    slot_blocks = []
    for slot_index in range(K_SLOTS):
        first = 2 * (positions[slot_index] - REACH) - parity + reach
        pair = lax.dynamic_slice_in_dim(halves, first, 2, 0)
        slot_blocks.append(pair.reshape(block_width, days_dev + LMAX))
    raw = jnp.concatenate([extended] + slot_blocks, 0)
    values = raw.astype(jnp.float32)
    shard_mean = jnp.mean(values[:, :days_dev], axis=1)
    shard_square = jnp.sum(jnp.square(values[:, :days_dev] - shard_mean[:, None]), axis=1)
    stats = lax.all_gather(jnp.stack([shard_mean, shard_square], 0), "tm")
    means, squares = stats[:, 0], stats[:, 1]
    point_mean = jnp.mean(means, axis=0)
    point_m2 = jnp.sum(squares, axis=0) + days_dev * jnp.sum(
        jnp.square(means - point_mean[None, :]), axis=0
    )
    spread = jnp.sqrt(point_m2 / total_days + 1e-06)
    day = lax.broadcasted_iota(jnp.int32, (1, days_dev + LMAX), 1)
    inside = (day < days_dev) | (lax.axis_index("tm") < tm_size - 1)
    standardized = jnp.where(
        inside, (values - point_mean[:, None]) / spread[:, None], 0.0
    ).astype(jnp.bfloat16)
    own = standardized[:half_rows]

    padded = jnp.concatenate(
        [
            jnp.zeros((half_rows, LMAX), jnp.bfloat16),
            own[:, :days_dev],
            jnp.zeros((half_rows, LMAX), jnp.bfloat16),
        ],
        1,
    )
    left_rows = []
    for lag_index in range(NLAG):
        lag_days = lag_set[lag_index]
        left_rows.append(
            jnp.concatenate(
                [
                    lax.dynamic_slice_in_dim(padded, LMAX - lag_days, days_dev + LMAX, 1),
                    lax.dynamic_slice_in_dim(own, lag_days, days_dev, 1),
                ],
                1,
            )
        )
    left = jnp.stack(left_rows, 1).reshape(half_rows * NLAG, -1)
    right_rows = []
    for slot_index in range(K_SLOTS):
        columns = standardized[half_rows + slot_index * block_width:][:block_width]
        right_rows.append(jnp.concatenate([columns, columns[:, :days_dev]], 1))
    right = jnp.concatenate(right_rows, 0)
    product = lax.dot_general(
        left, right, (((1,), (1,)), ((), ())), preferred_element_type=jnp.float32
    )

    out_rows = half_rows // tm_size
    comoment = lax.psum_scatter(product, "tm", scatter_dimension=0, tiled=True)
    comoment = comoment.reshape(out_rows, NLAG, K_SLOTS, block_width).transpose(0, 2, 1, 3)
    denominator = 2.0 * (total_days - lag_set).astype(jnp.float32)
    is_live = jnp.arange(K_SLOTS, dtype=jnp.int32) < live_count
    linked = jnp.where(
        is_live[None, :, None, None], comoment / denominator[None, None, :, None], 0.0
    )
    squares = jnp.sum(jnp.square(linked), axis=(1, 2, 3))
    row_scale = jnp.sqrt(squares / (live_count * NLAG * block_width).astype(jnp.float32) + 1e-06)
    return (linked / row_scale[:, None, None, None]).reshape(out_rows, -1)


def solution(mesh):
    return jax.shard_map(
        local,
        mesh=mesh,
        in_specs=(P("lon", "tm"), P(), P(), P()),
        out_specs=P(("lon", "tm"), None),
        check_vma=False,
    )
```

```python
import jax
import jax.numpy as jnp
from jax import lax
from jax.sharding import PartitionSpec as P

LMAX = 128
NLAG = 9
K_SLOTS = 3
REACH = 2


def shifted(value, axis, by):
    size = lax.axis_size(axis)
    pairs = [(i, i + by) for i in range(size) if 0 <= i + by < size]
    return lax.ppermute(value, axis, pairs)


def from_partner(value, axis, stride):
    mask = 2**stride
    pairs = [(source, source ^ mask) for source in range(lax.axis_size(axis))]
    return lax.ppermute(value, axis, pairs)


def shifted_2(value, axis, by):
    size = lax.axis_size(axis)
    return lax.ppermute(value, axis, [(i, (i + by) % size) for i in range(size)])


def dslice(value, start, size, axis):
    return lax.dynamic_slice_in_dim(value, start, size, axis, allow_negative_indices=False)


def local(anomalies, neighbor_ids, neighbor_counts, lag_set):
    half_rows, days_dev = anomalies.shape
    tm_size = lax.axis_size("tm")
    lon_size = lax.axis_size("lon")
    blocks = lon_size // 2
    block_width = 2 * half_rows
    total_days = days_dev * tm_size
    margin = shifted(anomalies[:, :LMAX], "tm", -1)
    extended = jnp.concatenate([anomalies, margin], 1)
    lon_index = lax.axis_index("lon")
    parity = lax.rem(lon_index, 2)
    block_index = lax.div(lon_index, 2)
    reach = 2 * REACH + 1
    halves = []
    for offset in range(-reach, reach + 1):
        if offset == 0:
            halves.append(extended)
            continue
        pairs = []
        for target in range(lon_size):
            low = -2 * REACH - target % 2
            if low <= offset <= low + 2 * (2 * REACH + 1) - 1:
                pairs.append(((target + offset) % lon_size, target))
        halves.append(lax.ppermute(extended, "lon", pairs))
    halves = jnp.stack(halves, 0)
    block_ids = dslice(neighbor_ids, block_index, 1, 0)[0]
    live_count = dslice(neighbor_counts, block_index, 1, 0)[0]
    positions = lax.rem(block_ids - block_index + (REACH + blocks), blocks)
    firsts = 2 * positions + (reach - 2 * REACH) - parity
    slot_blocks = []
    for slot_index in range(K_SLOTS):
        pair = dslice(halves, firsts[slot_index], 2, 0)
        slot_blocks.append(pair.reshape(block_width, days_dev + LMAX))
    raw = jnp.concatenate([extended] + slot_blocks, 0)
    values = raw.astype(jnp.float32)
    shard_mean = jnp.mean(values[:, :days_dev], axis=1)
    shard_square = jnp.sum(jnp.square(values[:, :days_dev] - shard_mean[:, None]), axis=1)
    stats = lax.all_gather(jnp.stack([shard_mean, shard_square], 0), "tm")
    means, squares = stats[:, 0], stats[:, 1]
    point_mean = jnp.mean(means, axis=0)
    point_m2 = jnp.sum(squares, axis=0) + days_dev * jnp.sum(
        jnp.square(means - point_mean[None, :]), axis=0
    )
    spread = jnp.sqrt(point_m2 / total_days + 1e-06)
    day = lax.broadcasted_iota(jnp.int32, (1, days_dev + LMAX), 1)
    inside = (day < days_dev) | (lax.axis_index("tm") < tm_size - 1)
    standardized = jnp.where(
        inside, (values - point_mean[:, None]) / spread[:, None], 0.0
    ).astype(jnp.bfloat16)
    own = standardized[:half_rows]

    padded = jnp.concatenate(
        [
            jnp.zeros((half_rows, LMAX), jnp.bfloat16),
            own[:, :days_dev],
            jnp.zeros((half_rows, LMAX), jnp.bfloat16),
        ],
        1,
    )
    backs = LMAX - lag_set
    left_rows = []
    for lag_index in range(NLAG):
        left_rows.append(
            jnp.concatenate(
                [
                    dslice(padded, backs[lag_index], days_dev + LMAX, 1),
                    dslice(own, lag_set[lag_index], days_dev, 1),
                ],
                1,
            )
        )
    left = jnp.stack(left_rows, 1).reshape(half_rows * NLAG, -1)
    right_rows = []
    for slot_index in range(K_SLOTS):
        columns = standardized[half_rows + slot_index * block_width:][:block_width]
        right_rows.append(jnp.concatenate([columns, columns[:, :days_dev]], 1))
    right = jnp.concatenate(right_rows, 0)
    product = lax.dot_general(
        left, right, (((1,), (1,)), ((), ())), preferred_element_type=jnp.float32
    )

    out_rows = half_rows // tm_size
    comoment = lax.psum_scatter(product, "tm", scatter_dimension=0, tiled=True)
    comoment = comoment.reshape(out_rows, NLAG, K_SLOTS, block_width).transpose(0, 2, 1, 3)
    denominator = 2.0 * (total_days - lag_set).astype(jnp.float32)
    is_live = jnp.arange(K_SLOTS, dtype=jnp.int32) < live_count
    linked = jnp.where(
        is_live[None, :, None, None], comoment / denominator[None, None, :, None], 0.0
    )
    squares = jnp.sum(jnp.square(linked), axis=(1, 2, 3))
    row_scale = jnp.sqrt(squares / (live_count * NLAG * block_width).astype(jnp.float32) + 1e-06)
    return (linked / row_scale[:, None, None, None]).reshape(out_rows, -1)


def solution(mesh):
    return jax.shard_map(
        local,
        mesh=mesh,
        in_specs=(P("lon", "tm"), P(), P(), P()),
        out_specs=P(("lon", "tm"), None),
        check_vma=False,
    )
```

```python
import jax
import jax.numpy as jnp
from jax import lax
from jax.sharding import PartitionSpec as P

LMAX = 128
NLAG = 9
K_SLOTS = 3
REACH = 2


def shifted(value, axis, by):
    size = lax.axis_size(axis)
    pairs = [(i, i + by) for i in range(size) if 0 <= i + by < size]
    return lax.ppermute(value, axis, pairs)


def from_partner(value, axis, stride):
    mask = 2**stride
    pairs = [(source, source ^ mask) for source in range(lax.axis_size(axis))]
    return lax.ppermute(value, axis, pairs)


def shifted_2(value, axis, by):
    size = lax.axis_size(axis)
    return lax.ppermute(value, axis, [(i, (i + by) % size) for i in range(size)])


def dslice(value, start, size, axis):
    return lax.dynamic_slice_in_dim(value, start, size, axis, allow_negative_indices=False)


def local(anomalies, neighbor_ids, neighbor_counts, lag_set):
    half_rows, days_dev = anomalies.shape
    tm_size = lax.axis_size("tm")
    lon_size = lax.axis_size("lon")
    blocks = lon_size // 2
    block_width = 2 * half_rows
    total_days = days_dev * tm_size
    margin = shifted(anomalies[:, :LMAX], "tm", -1)
    extended = jnp.concatenate([anomalies, margin], 1)
    lon_index = lax.axis_index("lon")
    parity = lax.rem(lon_index, 2)
    block_index = lax.div(lon_index, 2)
    reach = 2 * REACH + 1
    halves = []
    for offset in range(-reach, reach + 1):
        if offset == 0:
            halves.append(extended)
            continue
        pairs = []
        for target in range(lon_size):
            low = -2 * REACH - target % 2
            if low <= offset <= low + 2 * (2 * REACH + 1) - 1:
                pairs.append(((target + offset) % lon_size, target))
        halves.append(lax.ppermute(extended, "lon", pairs))
    halves = jnp.stack(halves, 0)
    block_ids = dslice(neighbor_ids, block_index, 1, 0)[0]
    live_count = dslice(neighbor_counts, block_index, 1, 0)[0]
    positions = lax.rem(block_ids - block_index + (REACH + blocks), blocks)
    firsts = 2 * positions + (reach - 2 * REACH) - parity
    slot_blocks = []
    for slot_index in range(K_SLOTS):
        pair = dslice(halves, firsts[slot_index], 2, 0)
        slot_blocks.append(pair.reshape(block_width, days_dev + LMAX))
    raw = jnp.concatenate([extended] + slot_blocks, 0)
    values = raw.astype(jnp.float32)
    shard_mean = jnp.mean(values[:, :days_dev], axis=1)
    shard_square = jnp.sum(jnp.square(values[:, :days_dev] - shard_mean[:, None]), axis=1)
    stats = lax.all_gather(jnp.stack([shard_mean, shard_square], 0), "tm")
    means, squares = stats[:, 0], stats[:, 1]
    point_mean = jnp.mean(means, axis=0)
    point_m2 = jnp.sum(squares, axis=0) + days_dev * jnp.sum(
        jnp.square(means - point_mean[None, :]), axis=0
    )
    spread = jnp.sqrt(point_m2 / total_days + 1e-06)
    day = lax.broadcasted_iota(jnp.int32, (1, days_dev + LMAX), 1)
    inside = (day < days_dev) | (lax.axis_index("tm") < tm_size - 1)
    standardized = jnp.where(
        inside, (values - point_mean[:, None]) / spread[:, None], 0.0
    ).astype(jnp.bfloat16)
    own = standardized[:half_rows]

    padded = jnp.concatenate(
        [
            jnp.zeros((half_rows, LMAX), jnp.bfloat16),
            own[:, :days_dev],
            jnp.zeros((half_rows, LMAX), jnp.bfloat16),
        ],
        1,
    )
    right_rows = []
    for slot_index in range(K_SLOTS):
        columns = standardized[half_rows + slot_index * block_width:][:block_width]
        right_rows.append(jnp.concatenate([columns, columns[:, :days_dev]], 1))
    right = jnp.concatenate(right_rows, 0)
    pieces = []
    for lag_index in range(NLAG):
        lag_days = lax.min(lag_set[lag_index], LMAX)
        left = jnp.concatenate(
            [
                dslice(padded, LMAX - lag_days, days_dev + LMAX, 1),
                dslice(own, lag_days, days_dev, 1),
            ],
            1,
        )
        pieces.append(
            lax.dot_general(
                left, right, (((1,), (1,)), ((), ())), preferred_element_type=jnp.float32
            )
        )
    product = jnp.concatenate(pieces, 1)

    out_rows = half_rows // tm_size
    comoment = lax.psum_scatter(product, "tm", scatter_dimension=0, tiled=True)
    comoment = comoment.reshape(out_rows, NLAG, K_SLOTS, block_width).transpose(0, 2, 1, 3)
    denominator = 2.0 * (total_days - lag_set).astype(jnp.float32)
    is_live = jnp.arange(K_SLOTS, dtype=jnp.int32) < live_count
    linked = jnp.where(
        is_live[None, :, None, None], comoment / denominator[None, None, :, None], 0.0
    )
    squares = jnp.sum(jnp.square(linked), axis=(1, 2, 3))
    row_scale = jnp.sqrt(squares / (live_count * NLAG * block_width).astype(jnp.float32) + 1e-06)
    return (linked / row_scale[:, None, None, None]).reshape(out_rows, -1)


def solution(mesh):
    return jax.shard_map(
        local,
        mesh=mesh,
        in_specs=(P("lon", "tm"), P(), P(), P()),
        out_specs=P(("lon", "tm"), None),
        check_vma=False,
    )
```

```python
import jax
import jax.numpy as jnp
from jax import lax
from jax.sharding import Mesh, PartitionSpec as P

LMAX = 128
NLAG = 9
K_SLOTS = 3
REACH = 2
TIME = ("tz", "tc")


def dslice(value, start, size, axis):
    return lax.dynamic_slice_in_dim(value, start, size, axis, allow_negative_indices=False)


def local(anomalies, neighbor_ids, neighbor_counts, lag_set):
    half_rows, days_dev = anomalies.shape
    tz_size = lax.axis_size("tz")
    tm_size = tz_size * lax.axis_size("tc")
    lon_size = lax.axis_size("lon")
    blocks = lon_size // 2
    block_width = 2 * half_rows
    total_days = days_dev * tm_size
    tm_index = lax.axis_index("tz") * 2 + lax.axis_index("tc")
    core = lax.axis_index("tc")
    margin = lax.ppermute(
        anomalies[:, :LMAX], TIME, [(i, i - 1) for i in range(1, tm_size)]
    )
    extended = jnp.concatenate([anomalies, margin], 1)
    lon_index = lax.axis_index("lon")
    parity = lax.rem(lon_index, 2)
    block_index = lax.div(lon_index, 2)
    reach = 2 * REACH + 1
    halves = []
    for offset in range(-reach, reach + 1):
        if offset == 0:
            halves.append(extended)
            continue
        pairs = []
        for target in range(lon_size):
            low = -2 * REACH - target % 2
            if low <= offset <= low + 2 * (2 * REACH + 1) - 1:
                pairs.append(((target + offset) % lon_size, target))
        halves.append(lax.ppermute(extended, "lon", pairs))
    halves = jnp.stack(halves, 0)
    block_ids = dslice(neighbor_ids, block_index, 1, 0)[0]
    live_count = dslice(neighbor_counts, block_index, 1, 0)[0]
    positions = lax.rem(block_ids - block_index + (REACH + blocks), blocks)
    firsts = 2 * positions + (reach - 2 * REACH) - parity
    slot_blocks = []
    for slot_index in range(K_SLOTS):
        pair = dslice(halves, firsts[slot_index], 2, 0)
        slot_blocks.append(pair.reshape(block_width, days_dev + LMAX))
    raw = jnp.concatenate([extended] + slot_blocks, 0)
    values = raw.astype(jnp.float32)
    shard_mean = jnp.mean(values[:, :days_dev], axis=1)
    shard_square = jnp.sum(jnp.square(values[:, :days_dev] - shard_mean[:, None]), axis=1)
    stats = lax.all_gather(jnp.stack([shard_mean, shard_square], 0), TIME)
    means, squares = stats[:, 0], stats[:, 1]
    point_mean = jnp.mean(means, axis=0)
    point_m2 = jnp.sum(squares, axis=0) + days_dev * jnp.sum(
        jnp.square(means - point_mean[None, :]), axis=0
    )
    spread = jnp.sqrt(point_m2 / total_days + 1e-06)
    day = lax.broadcasted_iota(jnp.int32, (1, days_dev + LMAX), 1)
    inside = (day < days_dev) | (tm_index < tm_size - 1)
    standardized = jnp.where(
        inside, (values - point_mean[:, None]) / spread[:, None], 0.0
    ).astype(jnp.bfloat16)

    other = lax.ppermute(standardized, "tc", [(0, 1), (1, 0)])
    first = core == 0
    window = jnp.concatenate(
        [
            jnp.where(first, standardized[:, :days_dev], other[:, :days_dev]),
            jnp.where(first, other, standardized),
        ],
        1,
    )
    span = 2 * days_dev
    out_rows = half_rows // tm_size
    own = window[:half_rows].reshape(tz_size, 2, out_rows, span + LMAX)
    own = dslice(own, core, 1, 1).reshape(half_rows // 2, span + LMAX)
    columns_all = window[half_rows:]

    padded = jnp.concatenate(
        [
            jnp.zeros((half_rows // 2, LMAX), jnp.bfloat16),
            own[:, :span],
            jnp.zeros((half_rows // 2, LMAX), jnp.bfloat16),
        ],
        1,
    )
    right_rows = []
    for slot_index in range(K_SLOTS):
        columns = columns_all[slot_index * block_width:][:block_width]
        right_rows.append(jnp.concatenate([columns, columns[:, :span]], 1))
    right = jnp.concatenate(right_rows, 0)
    pieces = []
    for lag_index in range(NLAG):
        lag_days = lax.min(lag_set[lag_index], LMAX)
        left = jnp.concatenate(
            [
                dslice(padded, LMAX - lag_days, span + LMAX, 1),
                dslice(own, lag_days, span, 1),
            ],
            1,
        )
        pieces.append(
            lax.dot_general(
                left, right, (((1,), (1,)), ((), ())), preferred_element_type=jnp.float32
            )
        )
    product = jnp.concatenate(pieces, 1)

    comoment = lax.psum_scatter(product, "tz", scatter_dimension=0, tiled=True)
    comoment = comoment.reshape(out_rows, NLAG, K_SLOTS, block_width).transpose(0, 2, 1, 3)
    denominator = 2.0 * (total_days - lag_set).astype(jnp.float32)
    is_live = jnp.arange(K_SLOTS, dtype=jnp.int32) < live_count
    linked = jnp.where(
        is_live[None, :, None, None], comoment / denominator[None, None, :, None], 0.0
    )
    squares = jnp.sum(jnp.square(linked), axis=(1, 2, 3))
    row_scale = jnp.sqrt(squares / (live_count * NLAG * block_width).astype(jnp.float32) + 1e-06)
    return (linked / row_scale[:, None, None, None]).reshape(out_rows, -1)


def solution(mesh):
    lon_size, tm_size = mesh.devices.shape
    split = Mesh(mesh.devices.reshape(lon_size, tm_size // 2, 2), ("lon", "tz", "tc"))
    return jax.shard_map(
        local,
        mesh=split,
        in_specs=(P("lon", TIME), P(), P(), P()),
        out_specs=P(("lon",) + TIME, None),
        check_vma=False,
    )
```

```python
import jax
import jax.numpy as jnp
from jax import lax
from jax.sharding import Mesh, PartitionSpec as P

LMAX = 128
NLAG = 9
K_SLOTS = 3
REACH = 2
TIME = ("tz", "tc")


def dslice(value, start, size, axis):
    return lax.dynamic_slice_in_dim(value, start, size, axis, allow_negative_indices=False)


def local(anomalies, neighbor_ids, neighbor_counts, lag_set):
    half_rows, days_dev = anomalies.shape
    tz_size = lax.axis_size("tz")
    tm_size = tz_size * lax.axis_size("tc")
    lon_size = lax.axis_size("lon")
    blocks = lon_size // 2
    block_width = 2 * half_rows
    total_days = days_dev * tm_size
    tm_index = lax.axis_index("tz") * 2 + lax.axis_index("tc")
    core = lax.axis_index("tc")
    margin = lax.ppermute(
        anomalies[:, :LMAX], TIME, [(i, i - 1) for i in range(1, tm_size)]
    )
    extended = jnp.concatenate([anomalies, margin], 1)
    lon_index = lax.axis_index("lon")
    parity = lax.rem(lon_index, 2)
    block_index = lax.div(lon_index, 2)
    reach = 2 * REACH + 1
    halves = []
    for offset in range(-reach, reach + 1):
        if offset == 0:
            halves.append(extended)
            continue
        pairs = []
        for target in range(lon_size):
            low = -2 * REACH - target % 2
            if low <= offset <= low + 2 * (2 * REACH + 1) - 1:
                pairs.append(((target + offset) % lon_size, target))
        halves.append(lax.ppermute(extended, "lon", pairs))
    halves = jnp.stack(halves, 0)
    block_ids = dslice(neighbor_ids, block_index, 1, 0)[0]
    live_count = dslice(neighbor_counts, block_index, 1, 0)[0]
    positions = lax.rem(block_ids - block_index + (REACH + blocks), blocks)
    firsts = 2 * positions + (reach - 2 * REACH) - parity
    slot_blocks = []
    for slot_index in range(K_SLOTS):
        pair = dslice(halves, firsts[slot_index], 2, 0)
        slot_blocks.append(pair.reshape(block_width, days_dev + LMAX))
    raw = jnp.concatenate([extended] + slot_blocks, 0)
    values = raw.astype(jnp.float32)
    shard_mean = jnp.mean(values[:, :days_dev], axis=1)
    shard_square = jnp.sum(jnp.square(values[:, :days_dev] - shard_mean[:, None]), axis=1)
    stats = lax.all_gather(jnp.stack([shard_mean, shard_square], 0), TIME)
    means, squares = stats[:, 0], stats[:, 1]
    point_mean = jnp.mean(means, axis=0)
    point_m2 = jnp.sum(squares, axis=0) + days_dev * jnp.sum(
        jnp.square(means - point_mean[None, :]), axis=0
    )
    spread = jnp.sqrt(point_m2 / total_days + 1e-06)
    day = lax.broadcasted_iota(jnp.int32, (1, days_dev + LMAX), 1)
    inside = (day < days_dev) | (tm_index < tm_size - 1)
    standardized = jnp.where(
        inside, (values - point_mean[:, None]) / spread[:, None], 0.0
    ).astype(jnp.bfloat16)

    other = lax.ppermute(standardized, "tc", [(0, 1), (1, 0)])
    pair = jnp.stack([standardized, other], 0)
    earlier = dslice(pair, core, 1, 0)[0]
    later = dslice(pair, 1 - core, 1, 0)[0]
    span = 2 * days_dev
    out_rows = half_rows // tm_size
    own = jnp.concatenate([earlier[:half_rows, :days_dev], later[:half_rows]], 1)
    own = own.reshape(tz_size, 2, out_rows, span + LMAX)
    own = dslice(own, core, 1, 1).reshape(half_rows // 2, span + LMAX)

    padded = jnp.concatenate(
        [
            jnp.zeros((half_rows // 2, LMAX), jnp.bfloat16),
            own[:, :span],
            jnp.zeros((half_rows // 2, LMAX), jnp.bfloat16),
        ],
        1,
    )
    early_columns = earlier[half_rows:, :days_dev]
    late_columns = later[half_rows:]
    right = jnp.concatenate(
        [early_columns, late_columns, early_columns, late_columns[:, :days_dev]], 1
    )
    pieces = []
    for lag_index in range(NLAG):
        lag_days = lax.min(lag_set[lag_index], LMAX)
        left = jnp.concatenate(
            [
                dslice(padded, LMAX - lag_days, span + LMAX, 1),
                dslice(own, lag_days, span, 1),
            ],
            1,
        )
        pieces.append(
            lax.dot_general(
                left, right, (((1,), (1,)), ((), ())), preferred_element_type=jnp.float32
            )
        )
    product = jnp.concatenate(pieces, 1)

    comoment = lax.psum_scatter(product, "tz", scatter_dimension=0, tiled=True)
    comoment = comoment.reshape(out_rows, NLAG, K_SLOTS, block_width).transpose(0, 2, 1, 3)
    denominator = 2.0 * (total_days - lag_set).astype(jnp.float32)
    is_live = jnp.arange(K_SLOTS, dtype=jnp.int32) < live_count
    linked = jnp.where(
        is_live[None, :, None, None], comoment / denominator[None, None, :, None], 0.0
    )
    squares = jnp.sum(jnp.square(linked), axis=(1, 2, 3))
    row_scale = jnp.sqrt(squares / (live_count * NLAG * block_width).astype(jnp.float32) + 1e-06)
    return (linked / row_scale[:, None, None, None]).reshape(out_rows, -1)


def solution(mesh):
    lon_size, tm_size = mesh.devices.shape
    split = Mesh(mesh.devices.reshape(lon_size, tm_size // 2, 2), ("lon", "tz", "tc"))
    return jax.shard_map(
        local,
        mesh=split,
        in_specs=(P("lon", TIME), P(), P(), P()),
        out_specs=P(("lon",) + TIME, None),
        check_vma=False,
    )
```

```python
import jax
import jax.numpy as jnp
from jax import lax
from jax.sharding import Mesh, PartitionSpec as P

LMAX = 128
NLAG = 9
K_SLOTS = 3
REACH = 2
TIME = ("tz", "tc")


def dslice(value, start, size, axis):
    return lax.dynamic_slice_in_dim(value, start, size, axis, allow_negative_indices=False)


def local(anomalies, neighbor_ids, neighbor_counts, lag_set):
    half_rows, days_dev = anomalies.shape
    tz_size = lax.axis_size("tz")
    tm_size = tz_size * lax.axis_size("tc")
    lon_size = lax.axis_size("lon")
    blocks = lon_size // 2
    block_width = 2 * half_rows
    total_days = days_dev * tm_size
    core = lax.axis_index("tc")
    margin = lax.ppermute(
        anomalies[:, :LMAX], TIME, [(i, i - 1) for i in range(1, tm_size)]
    )
    extended = jnp.concatenate([anomalies, margin], 1)
    lon_index = lax.axis_index("lon")
    parity = lax.rem(lon_index, 2)
    block_index = lax.div(lon_index, 2)
    reach = 2 * REACH + 1
    halves = []
    for offset in range(-reach, reach + 1):
        if offset == 0:
            halves.append(extended)
            continue
        pairs = []
        for target in range(lon_size):
            low = -2 * REACH - target % 2
            if low <= offset <= low + 2 * (2 * REACH + 1) - 1:
                pairs.append(((target + offset) % lon_size, target))
        halves.append(lax.ppermute(extended, "lon", pairs))
    halves = jnp.stack(halves, 0)
    block_ids = dslice(neighbor_ids, block_index, 1, 0)[0]
    live_count = dslice(neighbor_counts, block_index, 1, 0)[0]
    positions = lax.rem(block_ids - block_index + (REACH + blocks), blocks)
    firsts = 2 * positions + (reach - 2 * REACH) - parity
    slot_blocks = []
    for slot_index in range(K_SLOTS):
        pair = dslice(halves, firsts[slot_index], 2, 0)
        slot_blocks.append(pair.reshape(block_width, days_dev + LMAX))
    raw = jnp.concatenate([extended] + slot_blocks, 0)
    other = lax.ppermute(raw, "tc", [(0, 1), (1, 0)])
    values = raw[:, :days_dev].astype(jnp.float32)
    shard_mean = jnp.mean(values, axis=1)
    shard_square = jnp.sum(jnp.square(values - shard_mean[:, None]), axis=1)
    stats = lax.all_gather(jnp.stack([shard_mean, shard_square], 0), TIME)
    means, squares = stats[:, 0], stats[:, 1]
    point_mean = jnp.mean(means, axis=0)
    point_m2 = jnp.sum(squares, axis=0) + days_dev * jnp.sum(
        jnp.square(means - point_mean[None, :]), axis=0
    )
    spread = jnp.sqrt(point_m2 / total_days + 1e-06)

    pair = jnp.stack([raw, other], 0)
    earlier = dslice(pair, core, 1, 0)[0]
    later = dslice(pair, 1 - core, 1, 0)[0]
    span = 2 * days_dev
    window = jnp.concatenate([earlier[:, :days_dev], later], 1).astype(jnp.float32)
    day = lax.broadcasted_iota(jnp.int32, (1, span + LMAX), 1)
    inside = (day < span) | (lax.axis_index("tz") < tz_size - 1)
    standardized = jnp.where(
        inside, (window - point_mean[:, None]) / spread[:, None], 0.0
    ).astype(jnp.bfloat16)
    out_rows = half_rows // tm_size
    own = standardized[:half_rows].reshape(tz_size, 2, out_rows, span + LMAX)
    own = dslice(own, core, 1, 1).reshape(half_rows // 2, span + LMAX)
    columns = standardized[half_rows:]

    padded = jnp.concatenate(
        [
            jnp.zeros((half_rows // 2, LMAX), jnp.bfloat16),
            own[:, :span],
            jnp.zeros((half_rows // 2, LMAX), jnp.bfloat16),
        ],
        1,
    )
    right = jnp.concatenate([columns, columns[:, :span]], 1)
    pieces = []
    for lag_index in range(NLAG):
        lag_days = lax.min(lag_set[lag_index], LMAX)
        left = jnp.concatenate(
            [
                dslice(padded, LMAX - lag_days, span + LMAX, 1),
                dslice(own, lag_days, span, 1),
            ],
            1,
        )
        pieces.append(
            lax.dot_general(
                left, right, (((1,), (1,)), ((), ())), preferred_element_type=jnp.float32
            )
        )
    product = jnp.concatenate(pieces, 1)

    comoment = lax.psum_scatter(product, "tz", scatter_dimension=0, tiled=True)
    comoment = comoment.reshape(out_rows, NLAG, K_SLOTS, block_width).transpose(0, 2, 1, 3)
    denominator = 2.0 * (total_days - lag_set).astype(jnp.float32)
    is_live = jnp.arange(K_SLOTS, dtype=jnp.int32) < live_count
    linked = jnp.where(
        is_live[None, :, None, None], comoment / denominator[None, None, :, None], 0.0
    )
    squares = jnp.sum(jnp.square(linked), axis=(1, 2, 3))
    row_scale = jnp.sqrt(squares / (live_count * NLAG * block_width).astype(jnp.float32) + 1e-06)
    return (linked / row_scale[:, None, None, None]).reshape(out_rows, -1)


def solution(mesh):
    lon_size, tm_size = mesh.devices.shape
    split = Mesh(mesh.devices.reshape(lon_size, tm_size // 2, 2), ("lon", "tz", "tc"))
    return jax.shard_map(
        local,
        mesh=split,
        in_specs=(P("lon", TIME), P(), P(), P()),
        out_specs=P(("lon",) + TIME, None),
        check_vma=False,
    )
```

```python
import jax
import jax.numpy as jnp
from jax import lax
from jax.sharding import Mesh, PartitionSpec as P

LMAX = 128
NLAG = 9
K_SLOTS = 3
REACH = 2
TIME = ("tz", "tc")


def dslice(value, start, size, axis):
    return lax.dynamic_slice_in_dim(value, start, size, axis, allow_negative_indices=False)


def local(anomalies, neighbor_ids, neighbor_counts, lag_set):
    half_rows, days_dev = anomalies.shape
    tz_size = lax.axis_size("tz")
    tm_size = tz_size * lax.axis_size("tc")
    blocks = lax.axis_size("ly") * lax.axis_size("lx") // 2
    block_width = 2 * half_rows
    total_days = days_dev * tm_size
    core = lax.axis_index("tc")
    margin = lax.ppermute(
        anomalies[:, :LMAX], TIME, [(i, i - 1) for i in range(1, tm_size)]
    )
    extended = jnp.concatenate([anomalies, margin], 1)
    row_size = lax.axis_size("lx")
    lx_index = lax.axis_index("lx")
    parity = lax.rem(lx_index, 2)
    block_index = lax.axis_index("ly") * (row_size // 2) + lax.div(lx_index, 2)
    row = lax.all_gather(extended, "lx")
    rows_size = lax.axis_size("ly")
    before = lax.ppermute(row, "ly", [(i, (i + 1) % rows_size) for i in range(rows_size)])
    after = lax.ppermute(row, "ly", [(i, (i - 1) % rows_size) for i in range(rows_size)])
    halves = jnp.concatenate([before, row, after], 0)
    block_ids = dslice(neighbor_ids, block_index, 1, 0)[0]
    live_count = dslice(neighbor_counts, block_index, 1, 0)[0]
    positions = lax.rem(block_ids - block_index + (REACH + blocks), blocks)
    firsts = 2 * (positions + lax.div(lx_index, 2) + (row_size // 2 - REACH))
    slot_blocks = []
    for slot_index in range(K_SLOTS):
        pair = dslice(halves, firsts[slot_index], 2, 0)
        slot_blocks.append(pair.reshape(block_width, days_dev + LMAX))
    raw = jnp.concatenate([extended] + slot_blocks, 0)
    other = lax.ppermute(raw, "tc", [(0, 1), (1, 0)])
    values = raw[:, :days_dev].astype(jnp.float32)
    shard_mean = jnp.mean(values, axis=1)
    shard_square = jnp.sum(jnp.square(values - shard_mean[:, None]), axis=1)
    stats = lax.all_gather(jnp.stack([shard_mean, shard_square], 0), TIME)
    means, squares = stats[:, 0], stats[:, 1]
    point_mean = jnp.mean(means, axis=0)
    point_m2 = jnp.sum(squares, axis=0) + days_dev * jnp.sum(
        jnp.square(means - point_mean[None, :]), axis=0
    )
    spread = jnp.sqrt(point_m2 / total_days + 1e-06)

    pair = jnp.stack([raw, other], 0)
    earlier = dslice(pair, core, 1, 0)[0]
    later = dslice(pair, 1 - core, 1, 0)[0]
    span = 2 * days_dev
    window = jnp.concatenate([earlier[:, :days_dev], later], 1).astype(jnp.float32)
    day = lax.broadcasted_iota(jnp.int32, (1, span + LMAX), 1)
    inside = (day < span) | (lax.axis_index("tz") < tz_size - 1)
    standardized = jnp.where(
        inside, (window - point_mean[:, None]) / spread[:, None], 0.0
    ).astype(jnp.bfloat16)
    out_rows = half_rows // tm_size
    own = standardized[:half_rows].reshape(tz_size, 2, out_rows, span + LMAX)
    own = dslice(own, core, 1, 1).reshape(half_rows // 2, span + LMAX)
    columns = standardized[half_rows:]

    padded = jnp.concatenate(
        [
            jnp.zeros((half_rows // 2, LMAX), jnp.bfloat16),
            own[:, :span],
            jnp.zeros((half_rows // 2, LMAX), jnp.bfloat16),
        ],
        1,
    )
    right = jnp.concatenate([columns, columns[:, :span]], 1)
    pieces = []
    for lag_index in range(NLAG):
        lag_days = lax.min(lag_set[lag_index], LMAX)
        left = jnp.concatenate(
            [
                dslice(padded, LMAX - lag_days, span + LMAX, 1),
                dslice(own, lag_days, span, 1),
            ],
            1,
        )
        pieces.append(
            lax.dot_general(
                left, right, (((1,), (1,)), ((), ())), preferred_element_type=jnp.float32
            )
        )
    product = jnp.concatenate(pieces, 1)

    comoment = lax.psum_scatter(product, "tz", scatter_dimension=0, tiled=True)
    comoment = comoment.reshape(out_rows, NLAG, K_SLOTS, block_width).transpose(0, 2, 1, 3)
    denominator = 2.0 * (total_days - lag_set).astype(jnp.float32)
    is_live = jnp.arange(K_SLOTS, dtype=jnp.int32) < live_count
    linked = jnp.where(
        is_live[None, :, None, None], comoment / denominator[None, None, :, None], 0.0
    )
    squares = jnp.sum(jnp.square(linked), axis=(1, 2, 3))
    row_scale = jnp.sqrt(squares / (live_count * NLAG * block_width).astype(jnp.float32) + 1e-06)
    return (linked / row_scale[:, None, None, None]).reshape(out_rows, -1)


def solution(mesh):
    lon_size, tm_size = mesh.devices.shape
    split = Mesh(
        mesh.devices.reshape(lon_size // 4, 4, tm_size // 2, 2), ("ly", "lx", "tz", "tc")
    )
    return jax.shard_map(
        local,
        mesh=split,
        in_specs=(P(("ly", "lx"), TIME), P(), P(), P()),
        out_specs=P(("ly", "lx") + TIME, None),
        check_vma=False,
    )
```

```python
import jax
import jax.numpy as jnp
from jax import lax
from jax.sharding import Mesh, PartitionSpec as P

LMAX = 128
NLAG = 9
K_SLOTS = 3
REACH = 2
TIME = ("tz", "tc")


def dslice(value, start, size, axis):
    return lax.dynamic_slice_in_dim(value, start, size, axis, allow_negative_indices=False)


def local(anomalies, neighbor_ids, neighbor_counts, lag_set):
    half_rows, days_dev = anomalies.shape
    tz_size = lax.axis_size("tz")
    tm_size = tz_size * lax.axis_size("tc")
    blocks = lax.axis_size("ly") * lax.axis_size("lx") // 2
    block_width = 2 * half_rows
    total_days = days_dev * tm_size
    core = lax.axis_index("tc")
    margin = lax.ppermute(
        anomalies[:, :LMAX], TIME, [(i, i - 1) for i in range(1, tm_size)]
    )
    extended = jnp.concatenate([anomalies, margin], 1)
    row_size = lax.axis_size("lx")
    lx_index = lax.axis_index("lx")
    parity = lax.rem(lx_index, 2)
    block_index = lax.axis_index("ly") * (row_size // 2) + lax.div(lx_index, 2)
    row = lax.all_gather(extended, "lx")
    rows_size = lax.axis_size("ly")
    before = lax.ppermute(row, "ly", [(i, (i + 1) % rows_size) for i in range(rows_size)])
    after = lax.ppermute(row, "ly", [(i, (i - 1) % rows_size) for i in range(rows_size)])
    halves = jnp.concatenate([before, row, after], 0)
    block_ids = dslice(neighbor_ids, block_index, 1, 0)[0]
    live_count = dslice(neighbor_counts, block_index, 1, 0)[0]
    positions = lax.rem(block_ids - block_index + (REACH + blocks), blocks)
    firsts = 2 * (positions + lax.div(lx_index, 2) + (row_size // 2 - REACH))
    slot_blocks = []
    for slot_index in range(K_SLOTS):
        pair = dslice(halves, firsts[slot_index], 2, 0)
        slot_blocks.append(pair.reshape(block_width, days_dev + LMAX))
    raw = jnp.concatenate([extended] + slot_blocks, 0)
    other = lax.ppermute(raw, "tc", [(0, 1), (1, 0)])
    values = raw[:, :days_dev].astype(jnp.float32)
    shard_mean = jnp.mean(values, axis=1)
    shard_square = jnp.sum(jnp.square(values - shard_mean[:, None]), axis=1)
    point_mean, point_m2 = shard_mean, shard_square
    count = days_dev
    steps = [("tc", 1)] + [("tz", 1 << bit) for bit in range(tz_size.bit_length() - 1)]
    for axis, stride in steps:
        size = lax.axis_size(axis)
        pairs = [(i, i ^ stride) for i in range(size)]
        theirs = lax.ppermute(jnp.stack([point_mean, point_m2], 0), axis, pairs)
        their_mean, their_m2 = theirs[0], theirs[1]
        delta = their_mean - point_mean
        point_mean = (point_mean + their_mean) * 0.5
        point_m2 = (point_m2 + their_m2) + delta * delta * (count * 0.5)
        count = 2 * count
    spread = jnp.sqrt(point_m2 / total_days + 1e-06)

    pair = jnp.stack([raw, other], 0)
    earlier = dslice(pair, core, 1, 0)[0]
    later = dslice(pair, 1 - core, 1, 0)[0]
    span = 2 * days_dev
    window = jnp.concatenate([earlier[:, :days_dev], later], 1).astype(jnp.float32)
    day = lax.broadcasted_iota(jnp.int32, (1, span + LMAX), 1)
    inside = (day < span) | (lax.axis_index("tz") < tz_size - 1)
    standardized = jnp.where(
        inside, (window - point_mean[:, None]) / spread[:, None], 0.0
    ).astype(jnp.bfloat16)
    out_rows = half_rows // tm_size
    own = standardized[:half_rows].reshape(tz_size, 2, out_rows, span + LMAX)
    own = dslice(own, core, 1, 1).reshape(half_rows // 2, span + LMAX)
    columns = standardized[half_rows:]

    padded = jnp.concatenate(
        [
            jnp.zeros((half_rows // 2, LMAX), jnp.bfloat16),
            own[:, :span],
            jnp.zeros((half_rows // 2, LMAX), jnp.bfloat16),
        ],
        1,
    )
    right = jnp.concatenate([columns, columns[:, :span]], 1)
    pieces = []
    for lag_index in range(NLAG):
        lag_days = lax.min(lag_set[lag_index], LMAX)
        left = jnp.concatenate(
            [
                dslice(padded, LMAX - lag_days, span + LMAX, 1),
                dslice(own, lag_days, span, 1),
            ],
            1,
        )
        pieces.append(
            lax.dot_general(
                left, right, (((1,), (1,)), ((), ())), preferred_element_type=jnp.float32
            )
        )
    product = jnp.concatenate(pieces, 1)

    comoment = lax.psum_scatter(product, "tz", scatter_dimension=0, tiled=True)
    comoment = comoment.reshape(out_rows, NLAG, K_SLOTS, block_width).transpose(0, 2, 1, 3)
    denominator = 2.0 * (total_days - lag_set).astype(jnp.float32)
    is_live = jnp.arange(K_SLOTS, dtype=jnp.int32) < live_count
    linked = jnp.where(
        is_live[None, :, None, None], comoment / denominator[None, None, :, None], 0.0
    )
    squares = jnp.sum(jnp.square(linked), axis=(1, 2, 3))
    row_scale = jnp.sqrt(squares / (live_count * NLAG * block_width).astype(jnp.float32) + 1e-06)
    return (linked / row_scale[:, None, None, None]).reshape(out_rows, -1)


def solution(mesh):
    lon_size, tm_size = mesh.devices.shape
    split = Mesh(
        mesh.devices.reshape(lon_size // 4, 4, tm_size // 2, 2), ("ly", "lx", "tz", "tc")
    )
    return jax.shard_map(
        local,
        mesh=split,
        in_specs=(P(("ly", "lx"), TIME), P(), P(), P()),
        out_specs=P(("ly", "lx") + TIME, None),
        check_vma=False,
    )
```

```python
import jax
import jax.numpy as jnp
from jax import lax
from jax.sharding import Mesh, PartitionSpec as P

LMAX = 128
NLAG = 9
K_SLOTS = 3
REACH = 2
TIME = ("tz", "tc")


def dslice(value, start, size, axis):
    return lax.dynamic_slice_in_dim(value, start, size, axis, allow_negative_indices=False)


def local(anomalies, neighbor_ids, neighbor_counts, lag_set):
    half_rows, days_dev = anomalies.shape
    tz_size = lax.axis_size("tz")
    tm_size = tz_size * lax.axis_size("tc")
    blocks = lax.axis_size("ly") * lax.axis_size("lx") // 2
    block_width = 2 * half_rows
    total_days = days_dev * tm_size
    core = lax.axis_index("tc")
    margin = lax.ppermute(
        anomalies[:, :LMAX], TIME, [(i, i - 1) for i in range(1, tm_size)]
    )
    extended = jnp.concatenate([anomalies, margin], 1)
    row_size = lax.axis_size("lx")
    lx_index = lax.axis_index("lx")
    parity = lax.rem(lx_index, 2)
    block_index = lax.axis_index("ly") * (row_size // 2) + lax.div(lx_index, 2)
    row = lax.all_gather(extended, "lx")
    rows_size = lax.axis_size("ly")
    before = lax.ppermute(row, "ly", [(i, (i + 1) % rows_size) for i in range(rows_size)])
    after = lax.ppermute(row, "ly", [(i, (i - 1) % rows_size) for i in range(rows_size)])
    halves = jnp.concatenate([before, row, after], 0)
    block_ids = dslice(neighbor_ids, block_index, 1, 0)[0]
    live_count = dslice(neighbor_counts, block_index, 1, 0)[0]
    positions = lax.rem(block_ids - block_index + (REACH + blocks), blocks)
    firsts = 2 * (positions + lax.div(lx_index, 2) + (row_size // 2 - REACH))
    slot_blocks = []
    for slot_index in range(K_SLOTS):
        pair = dslice(halves, firsts[slot_index], 2, 0)
        slot_blocks.append(pair.reshape(block_width, days_dev + LMAX))
    raw = jnp.concatenate([extended] + slot_blocks, 0)
    other = lax.ppermute(raw, "tc", [(0, 1), (1, 0)])
    values = raw[:, :days_dev].astype(jnp.float32)
    shard_mean = jnp.mean(values, axis=1)
    shard_square = jnp.sum(jnp.square(values - shard_mean[:, None]), axis=1)
    stats = lax.all_gather(jnp.stack([shard_mean, shard_square], 0), TIME)
    means, squares = stats[:, 0], stats[:, 1]
    point_mean = jnp.mean(means, axis=0)
    point_m2 = jnp.sum(squares, axis=0) + days_dev * jnp.sum(
        jnp.square(means - point_mean[None, :]), axis=0
    )
    spread = jnp.sqrt(point_m2 / total_days + 1e-06)

    pair = jnp.stack([raw, other], 0)
    earlier = dslice(pair, core, 1, 0)[0]
    later = dslice(pair, 1 - core, 1, 0)[0]
    span = 2 * days_dev
    window = jnp.concatenate([earlier[:, :days_dev], later], 1).astype(jnp.float32)
    day = lax.broadcasted_iota(jnp.int32, (1, span + LMAX), 1)
    inside = (day < span) | (lax.axis_index("tz") < tz_size - 1)
    standardized = jnp.where(
        inside, (window - point_mean[:, None]) / spread[:, None], 0.0
    ).astype(jnp.bfloat16)
    out_rows = half_rows // tm_size
    own = standardized[:half_rows].reshape(tz_size, 2, out_rows, span + LMAX)
    own = dslice(own, core, 1, 1).reshape(half_rows // 2, span + LMAX)
    columns = standardized[half_rows:]

    padded = jnp.concatenate(
        [
            jnp.zeros((half_rows // 2, LMAX), jnp.bfloat16),
            own[:, :span],
            jnp.zeros((half_rows // 2, LMAX), jnp.bfloat16),
        ],
        1,
    )
    right = jnp.concatenate([columns, columns[:, :span]], 1)
    pieces = []
    for lag_index in range(NLAG):
        lag_days = lax.min(lag_set[lag_index], LMAX)
        left = jnp.concatenate(
            [
                dslice(padded, LMAX - lag_days, span + LMAX, 1),
                dslice(own, lag_days, span, 1),
            ],
            1,
        )
        pieces.append(
            lax.dot_general(
                left, right, (((1,), (1,)), ((), ())), preferred_element_type=jnp.float32
            )
        )
    parts = [
        lax.psum_scatter(
            jnp.concatenate(pieces[first:first + 3], 1), "tz", scatter_dimension=0, tiled=True
        )
        for first in range(0, NLAG, 3)
    ]
    comoment = jnp.concatenate(parts, 1)
    comoment = comoment.reshape(out_rows, NLAG, K_SLOTS, block_width).transpose(0, 2, 1, 3)
    denominator = 2.0 * (total_days - lag_set).astype(jnp.float32)
    is_live = jnp.arange(K_SLOTS, dtype=jnp.int32) < live_count
    linked = jnp.where(
        is_live[None, :, None, None], comoment / denominator[None, None, :, None], 0.0
    )
    squares = jnp.sum(jnp.square(linked), axis=(1, 2, 3))
    row_scale = jnp.sqrt(squares / (live_count * NLAG * block_width).astype(jnp.float32) + 1e-06)
    return (linked / row_scale[:, None, None, None]).reshape(out_rows, -1)


def solution(mesh):
    lon_size, tm_size = mesh.devices.shape
    split = Mesh(
        mesh.devices.reshape(lon_size // 4, 4, tm_size // 2, 2), ("ly", "lx", "tz", "tc")
    )
    return jax.shard_map(
        local,
        mesh=split,
        in_specs=(P(("ly", "lx"), TIME), P(), P(), P()),
        out_specs=P(("ly", "lx") + TIME, None),
        check_vma=False,
    )
```

```python
import jax
import jax.numpy as jnp
from jax import lax
from jax.sharding import Mesh, PartitionSpec as P

LMAX = 128
NLAG = 9
K_SLOTS = 3
REACH = 2
TIME = ("tz", "tc")


def dslice(value, start, size, axis):
    return lax.dynamic_slice_in_dim(value, start, size, axis, allow_negative_indices=False)


def local(anomalies, neighbor_ids, neighbor_counts, lag_set):
    half_rows, days_dev = anomalies.shape
    tz_size = lax.axis_size("tz")
    tm_size = tz_size * lax.axis_size("tc")
    blocks = lax.axis_size("ly") * lax.axis_size("lx") // 2
    block_width = 2 * half_rows
    total_days = days_dev * tm_size
    core = lax.axis_index("tc")
    margin = lax.ppermute(
        anomalies[:, :LMAX], TIME, [(i, i - 1) for i in range(1, tm_size)]
    )
    extended = jnp.concatenate([anomalies, margin], 1)
    row_size = lax.axis_size("lx")
    lx_index = lax.axis_index("lx")
    parity = lax.rem(lx_index, 2)
    block_index = lax.axis_index("ly") * (row_size // 2) + lax.div(lx_index, 2)
    row = lax.all_gather(extended, "lx")
    rows_size = lax.axis_size("ly")
    before = lax.ppermute(row, "ly", [(i, (i + 1) % rows_size) for i in range(rows_size)])
    after = lax.ppermute(row, "ly", [(i, (i - 1) % rows_size) for i in range(rows_size)])
    halves = jnp.concatenate([before, row, after], 0)
    block_ids = dslice(neighbor_ids, block_index, 1, 0)[0]
    live_count = dslice(neighbor_counts, block_index, 1, 0)[0]
    positions = lax.rem(block_ids - block_index + (REACH + blocks), blocks)
    firsts = 2 * (positions + lax.div(lx_index, 2) + (row_size // 2 - REACH))
    slot_blocks = []
    for slot_index in range(K_SLOTS):
        pair = dslice(halves, firsts[slot_index], 2, 0)
        slot_blocks.append(pair.reshape(block_width, days_dev + LMAX))
    raw = jnp.concatenate([extended] + slot_blocks, 0)
    other = lax.ppermute(raw, "tc", [(0, 1), (1, 0)])
    values = raw[:, :days_dev].astype(jnp.float32)
    shard_mean = jnp.mean(values, axis=1)
    shard_square = jnp.sum(jnp.square(values - shard_mean[:, None]), axis=1)
    stats = lax.all_gather(jnp.stack([shard_mean, shard_square], 0), TIME)
    means, squares = stats[:, 0], stats[:, 1]
    point_mean = jnp.mean(means, axis=0)
    point_m2 = jnp.sum(squares, axis=0) + days_dev * jnp.sum(
        jnp.square(means - point_mean[None, :]), axis=0
    )
    spread = jnp.sqrt(point_m2 / total_days + 1e-06)

    pair = jnp.stack([raw, other], 0)
    earlier = dslice(pair, core, 1, 0)[0]
    later = dslice(pair, 1 - core, 1, 0)[0]
    span = 2 * days_dev
    window = jnp.concatenate([earlier[:, :days_dev], later], 1).astype(jnp.float32)
    day = lax.broadcasted_iota(jnp.int32, (1, span + LMAX), 1)
    inside = (day < span) | (lax.axis_index("tz") < tz_size - 1)
    standardized = jnp.where(
        inside, (window - point_mean[:, None]) / spread[:, None], 0.0
    ).astype(jnp.bfloat16)
    out_rows = half_rows // tm_size
    own = standardized[:half_rows].reshape(tz_size, 2, out_rows, span + LMAX)
    own = dslice(own, core, 1, 1).reshape(half_rows // 2, span + LMAX)
    columns = standardized[half_rows:]

    padded = jnp.concatenate(
        [
            jnp.zeros((half_rows // 2, LMAX), jnp.bfloat16),
            own[:, :span],
            jnp.zeros((half_rows // 2, LMAX), jnp.bfloat16),
        ],
        1,
    )
    right = jnp.concatenate([columns, columns[:, :span]], 1)
    pieces = []
    for lag_index in range(NLAG):
        lag_days = lax.min(lag_set[lag_index], LMAX)
        left = jnp.concatenate(
            [
                dslice(padded, LMAX - lag_days, span + LMAX, 1),
                dslice(own, lag_days, span, 1),
            ],
            1,
        )
        pieces.append(
            lax.dot_general(
                left, right, (((1,), (1,)), ((), ())), preferred_element_type=jnp.float32
            )
        )
    product = jnp.concatenate(pieces, 1)

    received = lax.all_to_all(product, "tz", 0, 0, tiled=True)
    comoment = jnp.sum(received.reshape(tz_size, out_rows, -1), axis=0)
    comoment = comoment.reshape(out_rows, NLAG, K_SLOTS, block_width).transpose(0, 2, 1, 3)
    denominator = 2.0 * (total_days - lag_set).astype(jnp.float32)
    is_live = jnp.arange(K_SLOTS, dtype=jnp.int32) < live_count
    linked = jnp.where(
        is_live[None, :, None, None], comoment / denominator[None, None, :, None], 0.0
    )
    squares = jnp.sum(jnp.square(linked), axis=(1, 2, 3))
    row_scale = jnp.sqrt(squares / (live_count * NLAG * block_width).astype(jnp.float32) + 1e-06)
    return (linked / row_scale[:, None, None, None]).reshape(out_rows, -1)


def solution(mesh):
    lon_size, tm_size = mesh.devices.shape
    split = Mesh(
        mesh.devices.reshape(lon_size // 4, 4, tm_size // 2, 2), ("ly", "lx", "tz", "tc")
    )
    return jax.shard_map(
        local,
        mesh=split,
        in_specs=(P(("ly", "lx"), TIME), P(), P(), P()),
        out_specs=P(("ly", "lx") + TIME, None),
        check_vma=False,
    )
```

```python
import jax
import jax.numpy as jnp
from jax import lax
from jax.sharding import Mesh, PartitionSpec as P

LMAX = 128
NLAG = 9
K_SLOTS = 3
REACH = 2
TIME = ("tz", "tc")


def dslice(value, start, size, axis):
    return lax.dynamic_slice_in_dim(value, start, size, axis, allow_negative_indices=False)


def local(anomalies, neighbor_ids, neighbor_counts, lag_set):
    half_rows, days_dev = anomalies.shape
    tz_size = lax.axis_size("tz")
    tm_size = tz_size * lax.axis_size("tc")
    blocks = lax.axis_size("ly") * lax.axis_size("lx") // 2
    block_width = 2 * half_rows
    total_days = days_dev * tm_size
    core = lax.axis_index("tc")
    margin = lax.ppermute(
        anomalies[:, :LMAX], TIME, [(i, i - 1) for i in range(1, tm_size)]
    )
    extended = jnp.concatenate([anomalies, margin], 1)
    row_size = lax.axis_size("lx")
    lx_index = lax.axis_index("lx")
    parity = lax.rem(lx_index, 2)
    block_index = lax.axis_index("ly") * (row_size // 2) + lax.div(lx_index, 2)
    row = lax.all_gather(extended, "lx")
    rows_size = lax.axis_size("ly")
    before = lax.ppermute(row, "ly", [(i, (i + 1) % rows_size) for i in range(rows_size)])
    after = lax.ppermute(row, "ly", [(i, (i - 1) % rows_size) for i in range(rows_size)])
    halves = jnp.concatenate([before, row, after], 0)
    block_ids = dslice(neighbor_ids, block_index, 1, 0)[0]
    live_count = dslice(neighbor_counts, block_index, 1, 0)[0]
    positions = lax.rem(block_ids - block_index + (REACH + blocks), blocks)
    firsts = 2 * (positions + lax.div(lx_index, 2) + (row_size // 2 - REACH))
    slot_blocks = []
    for slot_index in range(K_SLOTS):
        pair = dslice(halves, firsts[slot_index], 2, 0)
        slot_blocks.append(pair.reshape(block_width, days_dev + LMAX))
    raw = jnp.concatenate([extended] + slot_blocks, 0)
    other = lax.ppermute(raw, "tc", [(0, 1), (1, 0)])
    values = raw[:, :days_dev].astype(jnp.float32)
    shard_mean = jnp.mean(values, axis=1)
    shard_square = jnp.sum(jnp.square(values - shard_mean[:, None]), axis=1)
    stats = lax.all_gather(jnp.stack([shard_mean, shard_square], 0), TIME)
    means, squares = stats[:, 0], stats[:, 1]
    point_mean = jnp.mean(means, axis=0)
    point_m2 = jnp.sum(squares, axis=0) + days_dev * jnp.sum(
        jnp.square(means - point_mean[None, :]), axis=0
    )
    spread = jnp.sqrt(point_m2 / total_days + 1e-06)

    pair = jnp.stack([raw, other], 0)
    earlier = dslice(pair, core, 1, 0)[0]
    later = dslice(pair, 1 - core, 1, 0)[0]
    span = 2 * days_dev
    window = jnp.concatenate([earlier[:, :days_dev], later], 1).astype(jnp.float32)
    day = lax.broadcasted_iota(jnp.int32, (1, span + LMAX), 1)
    inside = (day < span) | (lax.axis_index("tz") < tz_size - 1)
    standardized = jnp.where(
        inside, (window - point_mean[:, None]) / spread[:, None], 0.0
    ).astype(jnp.bfloat16)
    out_rows = half_rows // tm_size
    own = standardized[:half_rows].reshape(tz_size, 2, out_rows, span + LMAX)
    own = dslice(own, core, 1, 1).reshape(half_rows // 2, span + LMAX)
    columns = standardized[half_rows:]

    padded = jnp.concatenate(
        [
            jnp.zeros((half_rows // 2, LMAX), jnp.bfloat16),
            own[:, :span],
            jnp.zeros((half_rows // 2, LMAX), jnp.bfloat16),
        ],
        1,
    )
    right = jnp.concatenate([columns, columns[:, :span]], 1)
    pieces = []
    for lag_index in range(NLAG):
        lag_days = lax.min(lag_set[lag_index], LMAX)
        left = jnp.concatenate(
            [
                dslice(padded, LMAX - lag_days, span + LMAX, 1),
                dslice(own, lag_days, span, 1),
            ],
            1,
        )
        pieces.append(
            lax.dot_general(
                left, right, (((1,), (1,)), ((), ())), preferred_element_type=jnp.float32
            )
        )
    early = 5
    scattered = lax.psum_scatter(
        jnp.concatenate(pieces[:early], 1), "tz", scatter_dimension=0, tiled=True
    )
    received = lax.all_to_all(jnp.concatenate(pieces[early:], 1), "tz", 0, 0, tiled=True)
    summed = jnp.sum(received.reshape(tz_size, out_rows, -1), axis=0)
    comoment = jnp.concatenate([scattered, summed], 1)
    comoment = comoment.reshape(out_rows, NLAG, K_SLOTS, block_width).transpose(0, 2, 1, 3)
    denominator = 2.0 * (total_days - lag_set).astype(jnp.float32)
    is_live = jnp.arange(K_SLOTS, dtype=jnp.int32) < live_count
    linked = jnp.where(
        is_live[None, :, None, None], comoment / denominator[None, None, :, None], 0.0
    )
    squares = jnp.sum(jnp.square(linked), axis=(1, 2, 3))
    row_scale = jnp.sqrt(squares / (live_count * NLAG * block_width).astype(jnp.float32) + 1e-06)
    return (linked / row_scale[:, None, None, None]).reshape(out_rows, -1)


def solution(mesh):
    lon_size, tm_size = mesh.devices.shape
    split = Mesh(
        mesh.devices.reshape(lon_size // 4, 4, tm_size // 2, 2), ("ly", "lx", "tz", "tc")
    )
    return jax.shard_map(
        local,
        mesh=split,
        in_specs=(P(("ly", "lx"), TIME), P(), P(), P()),
        out_specs=P(("ly", "lx") + TIME, None),
        check_vma=False,
    )
```

```python
import jax
import jax.numpy as jnp
from jax import lax
from jax.sharding import Mesh, PartitionSpec as P

LMAX = 128
NLAG = 9
K_SLOTS = 3
REACH = 2
TIME = ("tz", "tc")


def dslice(value, start, size, axis):
    return lax.dynamic_slice_in_dim(value, start, size, axis, allow_negative_indices=False)


def local(anomalies, neighbor_ids, neighbor_counts, lag_set):
    half_rows, days_dev = anomalies.shape
    tz_size = lax.axis_size("tz")
    tm_size = tz_size * lax.axis_size("tc")
    blocks = lax.axis_size("ly") * lax.axis_size("lx") // 2
    block_width = 2 * half_rows
    total_days = days_dev * tm_size
    core = lax.axis_index("tc")
    margin = lax.ppermute(
        anomalies[:, :LMAX], TIME, [(i, i - 1) for i in range(1, tm_size)]
    )
    extended = jnp.concatenate([anomalies, margin], 1)
    row_size = lax.axis_size("lx")
    lx_index = lax.axis_index("lx")
    parity = lax.rem(lx_index, 2)
    block_index = lax.axis_index("ly") * (row_size // 2) + lax.div(lx_index, 2)
    row = lax.all_gather(extended, "lx")
    rows_size = lax.axis_size("ly")
    before = lax.ppermute(row, "ly", [(i, (i + 1) % rows_size) for i in range(rows_size)])
    after = lax.ppermute(row, "ly", [(i, (i - 1) % rows_size) for i in range(rows_size)])
    halves = jnp.concatenate([before, row, after], 0)
    block_ids = dslice(neighbor_ids, block_index, 1, 0)[0]
    live_count = dslice(neighbor_counts, block_index, 1, 0)[0]
    positions = lax.rem(block_ids - block_index + (REACH + blocks), blocks)
    firsts = 2 * (positions + lax.div(lx_index, 2) + (row_size // 2 - REACH))
    slot_blocks = []
    for slot_index in range(K_SLOTS):
        pair = dslice(halves, firsts[slot_index], 2, 0)
        slot_blocks.append(pair.reshape(block_width, days_dev + LMAX))
    raw = jnp.concatenate([extended] + slot_blocks, 0)
    other = lax.ppermute(raw, "tc", [(0, 1), (1, 0)])
    values = raw[:, :days_dev].astype(jnp.float32)
    shard_mean = jnp.mean(values, axis=1)
    shard_square = jnp.sum(jnp.square(values - shard_mean[:, None]), axis=1)
    stats = lax.all_gather(jnp.stack([shard_mean, shard_square], 0), TIME)
    means, squares = stats[:, 0], stats[:, 1]
    point_mean = jnp.mean(means, axis=0)
    point_m2 = jnp.sum(squares, axis=0) + days_dev * jnp.sum(
        jnp.square(means - point_mean[None, :]), axis=0
    )
    spread = jnp.sqrt(point_m2 / total_days + 1e-06)

    pair = jnp.stack([raw, other], 0)
    earlier = dslice(pair, core, 1, 0)[0]
    later = dslice(pair, 1 - core, 1, 0)[0]
    span = 2 * days_dev
    window = jnp.concatenate([earlier[:, :days_dev], later], 1).astype(jnp.float32)
    day = lax.broadcasted_iota(jnp.int32, (1, span + LMAX), 1)
    inside = (day < span) | (lax.axis_index("tz") < tz_size - 1)
    standardized = jnp.where(
        inside, (window - point_mean[:, None]) / spread[:, None], 0.0
    ).astype(jnp.bfloat16)
    out_rows = half_rows // tm_size
    own = standardized[:half_rows].reshape(tz_size, 2, out_rows, span + LMAX)
    own = dslice(own, core, 1, 1).reshape(half_rows // 2, span + LMAX)
    columns = standardized[half_rows:]

    padded = jnp.concatenate(
        [
            jnp.zeros((half_rows // 2, LMAX), jnp.bfloat16),
            own[:, :span],
            jnp.zeros((half_rows // 2, LMAX), jnp.bfloat16),
        ],
        1,
    )
    right = jnp.concatenate([columns, columns[:, :span]], 1)
    pieces = []
    for lag_index in range(NLAG):
        lag_days = lax.min(lag_set[lag_index], LMAX)
        left = jnp.concatenate(
            [
                dslice(padded, LMAX - lag_days, span + LMAX, 1),
                dslice(own, lag_days, span, 1),
            ],
            1,
        )
        pieces.append(
            lax.dot_general(
                left, right, (((1,), (1,)), ((), ())), preferred_element_type=jnp.float32
            )
        )
    early = 5
    sums = []
    for part in (pieces[:early], pieces[early:]):
        received = lax.all_to_all(jnp.concatenate(part, 1), "tz", 0, 0, tiled=True)
        sums.append(jnp.sum(received.reshape(tz_size, out_rows, -1), axis=0))
    comoment = jnp.concatenate(sums, 1)
    comoment = comoment.reshape(out_rows, NLAG, K_SLOTS, block_width).transpose(0, 2, 1, 3)
    denominator = 2.0 * (total_days - lag_set).astype(jnp.float32)
    is_live = jnp.arange(K_SLOTS, dtype=jnp.int32) < live_count
    linked = jnp.where(
        is_live[None, :, None, None], comoment / denominator[None, None, :, None], 0.0
    )
    squares = jnp.sum(jnp.square(linked), axis=(1, 2, 3))
    row_scale = jnp.sqrt(squares / (live_count * NLAG * block_width).astype(jnp.float32) + 1e-06)
    return (linked / row_scale[:, None, None, None]).reshape(out_rows, -1)


def solution(mesh):
    lon_size, tm_size = mesh.devices.shape
    split = Mesh(
        mesh.devices.reshape(lon_size // 4, 4, tm_size // 2, 2), ("ly", "lx", "tz", "tc")
    )
    return jax.shard_map(
        local,
        mesh=split,
        in_specs=(P(("ly", "lx"), TIME), P(), P(), P()),
        out_specs=P(("ly", "lx") + TIME, None),
        check_vma=False,
    )
```

```python
import jax
import jax.numpy as jnp
from jax import lax
from jax.sharding import Mesh, PartitionSpec as P

LMAX = 128
NLAG = 9
K_SLOTS = 3
REACH = 2
TIME = ("tz", "tc")


def dslice(value, start, size, axis):
    return lax.dynamic_slice_in_dim(value, start, size, axis, allow_negative_indices=False)


def local(anomalies, neighbor_ids, neighbor_counts, lag_set):
    half_rows, days_dev = anomalies.shape
    tz_size = lax.axis_size("tz")
    tm_size = tz_size * lax.axis_size("tc")
    blocks = lax.axis_size("ly") * lax.axis_size("lx") // 2
    block_width = 2 * half_rows
    total_days = days_dev * tm_size
    core = lax.axis_index("tc")
    margin = lax.ppermute(
        anomalies[:, :LMAX], TIME, [(i, i - 1) for i in range(1, tm_size)]
    )
    extended = jnp.concatenate([anomalies, margin], 1)
    row_size = lax.axis_size("lx")
    lx_index = lax.axis_index("lx")
    parity = lax.rem(lx_index, 2)
    block_index = lax.axis_index("ly") * (row_size // 2) + lax.div(lx_index, 2)
    received = [extended] + [
        lax.ppermute(extended, "lx", [(i, (i - k) % row_size) for i in range(row_size)])
        for k in range(1, row_size)
    ]
    doubled = jnp.stack(received + received, 0)
    row = dslice(doubled, lax.rem(row_size - lx_index, row_size), row_size, 0)
    rows_size = lax.axis_size("ly")
    before = lax.ppermute(row, "ly", [(i, (i + 1) % rows_size) for i in range(rows_size)])
    after = lax.ppermute(row, "ly", [(i, (i - 1) % rows_size) for i in range(rows_size)])
    halves = jnp.concatenate([before, row, after], 0)
    block_ids = dslice(neighbor_ids, block_index, 1, 0)[0]
    live_count = dslice(neighbor_counts, block_index, 1, 0)[0]
    positions = lax.rem(block_ids - block_index + (REACH + blocks), blocks)
    firsts = 2 * (positions + lax.div(lx_index, 2) + (row_size // 2 - REACH))
    slot_blocks = []
    for slot_index in range(K_SLOTS):
        pair = dslice(halves, firsts[slot_index], 2, 0)
        slot_blocks.append(pair.reshape(block_width, days_dev + LMAX))
    raw = jnp.concatenate([extended] + slot_blocks, 0)
    other = lax.ppermute(raw, "tc", [(0, 1), (1, 0)])
    values = raw[:, :days_dev].astype(jnp.float32)
    shard_mean = jnp.mean(values, axis=1)
    shard_square = jnp.sum(jnp.square(values - shard_mean[:, None]), axis=1)
    stats = lax.all_gather(jnp.stack([shard_mean, shard_square], 0), TIME)
    means, squares = stats[:, 0], stats[:, 1]
    point_mean = jnp.mean(means, axis=0)
    point_m2 = jnp.sum(squares, axis=0) + days_dev * jnp.sum(
        jnp.square(means - point_mean[None, :]), axis=0
    )
    spread = jnp.sqrt(point_m2 / total_days + 1e-06)

    pair = jnp.stack([raw, other], 0)
    earlier = dslice(pair, core, 1, 0)[0]
    later = dslice(pair, 1 - core, 1, 0)[0]
    span = 2 * days_dev
    window = jnp.concatenate([earlier[:, :days_dev], later], 1).astype(jnp.float32)
    day = lax.broadcasted_iota(jnp.int32, (1, span + LMAX), 1)
    inside = (day < span) | (lax.axis_index("tz") < tz_size - 1)
    standardized = jnp.where(
        inside, (window - point_mean[:, None]) / spread[:, None], 0.0
    ).astype(jnp.bfloat16)
    out_rows = half_rows // tm_size
    own = standardized[:half_rows].reshape(tz_size, 2, out_rows, span + LMAX)
    own = dslice(own, core, 1, 1).reshape(half_rows // 2, span + LMAX)
    columns = standardized[half_rows:]

    padded = jnp.concatenate(
        [
            jnp.zeros((half_rows // 2, LMAX), jnp.bfloat16),
            own[:, :span],
            jnp.zeros((half_rows // 2, LMAX), jnp.bfloat16),
        ],
        1,
    )
    right = jnp.concatenate([columns, columns[:, :span]], 1)
    pieces = []
    for lag_index in range(NLAG):
        lag_days = lax.min(lag_set[lag_index], LMAX)
        left = jnp.concatenate(
            [
                dslice(padded, LMAX - lag_days, span + LMAX, 1),
                dslice(own, lag_days, span, 1),
            ],
            1,
        )
        pieces.append(
            lax.dot_general(
                left, right, (((1,), (1,)), ((), ())), preferred_element_type=jnp.float32
            )
        )
    product = jnp.concatenate(pieces, 1)

    received = lax.all_to_all(product, "tz", 0, 0, tiled=True)
    comoment = jnp.sum(received.reshape(tz_size, out_rows, -1), axis=0)
    comoment = comoment.reshape(out_rows, NLAG, K_SLOTS, block_width).transpose(0, 2, 1, 3)
    denominator = 2.0 * (total_days - lag_set).astype(jnp.float32)
    is_live = jnp.arange(K_SLOTS, dtype=jnp.int32) < live_count
    linked = jnp.where(
        is_live[None, :, None, None], comoment / denominator[None, None, :, None], 0.0
    )
    squares = jnp.sum(jnp.square(linked), axis=(1, 2, 3))
    row_scale = jnp.sqrt(squares / (live_count * NLAG * block_width).astype(jnp.float32) + 1e-06)
    return (linked / row_scale[:, None, None, None]).reshape(out_rows, -1)


def solution(mesh):
    lon_size, tm_size = mesh.devices.shape
    split = Mesh(
        mesh.devices.reshape(lon_size // 4, 4, tm_size // 2, 2), ("ly", "lx", "tz", "tc")
    )
    return jax.shard_map(
        local,
        mesh=split,
        in_specs=(P(("ly", "lx"), TIME), P(), P(), P()),
        out_specs=P(("ly", "lx") + TIME, None),
        check_vma=False,
    )
```

```python
import jax
import jax.numpy as jnp
from jax import lax
from jax.sharding import Mesh, PartitionSpec as P

LMAX = 128
NLAG = 9
K_SLOTS = 3
REACH = 2
TIME = ("tz", "tc")


def dslice(value, start, size, axis):
    return lax.dynamic_slice_in_dim(value, start, size, axis, allow_negative_indices=False)


def local(anomalies, neighbor_ids, neighbor_counts, lag_set):
    half_rows, days_dev = anomalies.shape
    tz_size = lax.axis_size("tz")
    tm_size = tz_size * lax.axis_size("tc")
    blocks = lax.axis_size("ly") * lax.axis_size("lx") // 2
    block_width = 2 * half_rows
    total_days = days_dev * tm_size
    core = lax.axis_index("tc")
    margin = lax.ppermute(
        anomalies[:, :LMAX], TIME, [(i, i - 1) for i in range(1, tm_size)]
    )
    extended = jnp.concatenate([anomalies, margin], 1)
    row_size = lax.axis_size("lx")
    lx_index = lax.axis_index("lx")
    parity = lax.rem(lx_index, 2)
    block_index = lax.axis_index("ly") * (row_size // 2) + lax.div(lx_index, 2)
    row = lax.all_gather(extended, "lx")
    rows_size = lax.axis_size("ly")
    before = lax.ppermute(row, "ly", [(i, (i + 1) % rows_size) for i in range(rows_size)])
    after = lax.ppermute(row, "ly", [(i, (i - 1) % rows_size) for i in range(rows_size)])
    halves = jnp.concatenate([before, row, after], 0)
    block_ids = dslice(neighbor_ids, block_index, 1, 0)[0]
    live_count = dslice(neighbor_counts, block_index, 1, 0)[0]
    positions = lax.rem(block_ids - block_index + (REACH + blocks), blocks)
    firsts = 2 * (positions + lax.div(lx_index, 2) + (row_size // 2 - REACH))
    slot_blocks = []
    for slot_index in range(K_SLOTS):
        pair = dslice(halves, firsts[slot_index], 2, 0)
        slot_blocks.append(pair.reshape(block_width, days_dev + LMAX))
    raw = jnp.concatenate([extended] + slot_blocks, 0)
    other = lax.ppermute(raw, "tc", [(0, 1), (1, 0)])
    values = raw[:, :days_dev].astype(jnp.float32)
    shard_mean = jnp.mean(values, axis=1)
    shard_square = jnp.sum(jnp.square(values - shard_mean[:, None]), axis=1)
    along = lax.all_gather(jnp.stack([shard_mean, shard_square], 0), "tz")
    across = lax.ppermute(along, "tc", [(0, 1), (1, 0)])
    ordered = jnp.stack([along, across], 0)
    stats = jnp.concatenate(
        [dslice(ordered, core, 1, 0)[0], dslice(ordered, 1 - core, 1, 0)[0]], 0
    )
    means, squares = stats[:, 0], stats[:, 1]
    point_mean = jnp.mean(means, axis=0)
    point_m2 = jnp.sum(squares, axis=0) + days_dev * jnp.sum(
        jnp.square(means - point_mean[None, :]), axis=0
    )
    spread = jnp.sqrt(point_m2 / total_days + 1e-06)

    pair = jnp.stack([raw, other], 0)
    earlier = dslice(pair, core, 1, 0)[0]
    later = dslice(pair, 1 - core, 1, 0)[0]
    span = 2 * days_dev
    window = jnp.concatenate([earlier[:, :days_dev], later], 1).astype(jnp.float32)
    day = lax.broadcasted_iota(jnp.int32, (1, span + LMAX), 1)
    inside = (day < span) | (lax.axis_index("tz") < tz_size - 1)
    standardized = jnp.where(
        inside, (window - point_mean[:, None]) / spread[:, None], 0.0
    ).astype(jnp.bfloat16)
    out_rows = half_rows // tm_size
    own = standardized[:half_rows].reshape(tz_size, 2, out_rows, span + LMAX)
    own = dslice(own, core, 1, 1).reshape(half_rows // 2, span + LMAX)
    columns = standardized[half_rows:]

    padded = jnp.concatenate(
        [
            jnp.zeros((half_rows // 2, LMAX), jnp.bfloat16),
            own[:, :span],
            jnp.zeros((half_rows // 2, LMAX), jnp.bfloat16),
        ],
        1,
    )
    right = jnp.concatenate([columns, columns[:, :span]], 1)
    pieces = []
    for lag_index in range(NLAG):
        lag_days = lax.min(lag_set[lag_index], LMAX)
        left = jnp.concatenate(
            [
                dslice(padded, LMAX - lag_days, span + LMAX, 1),
                dslice(own, lag_days, span, 1),
            ],
            1,
        )
        pieces.append(
            lax.dot_general(
                left, right, (((1,), (1,)), ((), ())), preferred_element_type=jnp.float32
            )
        )
    product = jnp.concatenate(pieces, 1)

    received = lax.all_to_all(product, "tz", 0, 0, tiled=True)
    comoment = jnp.sum(received.reshape(tz_size, out_rows, -1), axis=0)
    comoment = comoment.reshape(out_rows, NLAG, K_SLOTS, block_width).transpose(0, 2, 1, 3)
    denominator = 2.0 * (total_days - lag_set).astype(jnp.float32)
    is_live = jnp.arange(K_SLOTS, dtype=jnp.int32) < live_count
    linked = jnp.where(
        is_live[None, :, None, None], comoment / denominator[None, None, :, None], 0.0
    )
    squares = jnp.sum(jnp.square(linked), axis=(1, 2, 3))
    row_scale = jnp.sqrt(squares / (live_count * NLAG * block_width).astype(jnp.float32) + 1e-06)
    return (linked / row_scale[:, None, None, None]).reshape(out_rows, -1)


def solution(mesh):
    lon_size, tm_size = mesh.devices.shape
    split = Mesh(
        mesh.devices.reshape(lon_size // 4, 4, tm_size // 2, 2), ("ly", "lx", "tz", "tc")
    )
    return jax.shard_map(
        local,
        mesh=split,
        in_specs=(P(("ly", "lx"), TIME), P(), P(), P()),
        out_specs=P(("ly", "lx") + TIME, None),
        check_vma=False,
    )
```

```python
import jax
import jax.numpy as jnp
from jax import lax
from jax.sharding import Mesh, PartitionSpec as P

LMAX = 128
NLAG = 9
K_SLOTS = 3
REACH = 2
TIME = ("tz", "tc")


def dslice(value, start, size, axis):
    return lax.dynamic_slice_in_dim(value, start, size, axis, allow_negative_indices=False)


def local(anomalies, neighbor_ids, neighbor_counts, lag_set):
    half_rows, days_dev = anomalies.shape
    tz_size = lax.axis_size("tz")
    tm_size = tz_size * lax.axis_size("tc")
    blocks = lax.axis_size("ly") * lax.axis_size("lx") // 2
    block_width = 2 * half_rows
    total_days = days_dev * tm_size
    core = lax.axis_index("tc")
    margin = lax.ppermute(
        anomalies[:, :LMAX], TIME, [(i, i - 1) for i in range(1, tm_size)]
    )
    extended = jnp.concatenate([anomalies, margin], 1)
    row_size = lax.axis_size("lx")
    lx_index = lax.axis_index("lx")
    parity = lax.rem(lx_index, 2)
    block_index = lax.axis_index("ly") * (row_size // 2) + lax.div(lx_index, 2)
    row = lax.all_gather(extended, "lx")
    rows_size = lax.axis_size("ly")
    before = lax.ppermute(row, "ly", [(i, (i + 1) % rows_size) for i in range(rows_size)])
    after = lax.ppermute(row, "ly", [(i, (i - 1) % rows_size) for i in range(rows_size)])
    halves = jnp.concatenate([before, row, after], 0)
    block_ids = dslice(neighbor_ids, block_index, 1, 0)[0]
    live_count = dslice(neighbor_counts, block_index, 1, 0)[0]
    positions = lax.rem(block_ids - block_index + (REACH + blocks), blocks)
    firsts = 2 * (positions + lax.div(lx_index, 2) + (row_size // 2 - REACH))
    slot_blocks = []
    for slot_index in range(K_SLOTS):
        pair = dslice(halves, firsts[slot_index], 2, 0)
        slot_blocks.append(pair.reshape(block_width, days_dev + LMAX))
    raw = jnp.concatenate([extended] + slot_blocks, 0)
    other = lax.ppermute(raw, "tc", [(0, 1), (1, 0)])
    values = raw[:, :days_dev].astype(jnp.float32)
    shard_mean = jnp.mean(values, axis=1)
    shard_square = jnp.sum(jnp.square(values - shard_mean[:, None]), axis=1)
    stats = lax.all_gather(jnp.stack([shard_mean, shard_square], 0), TIME)
    means, squares = stats[:, 0], stats[:, 1]
    point_mean = jnp.mean(means, axis=0)
    point_m2 = jnp.sum(squares, axis=0) + days_dev * jnp.sum(
        jnp.square(means - point_mean[None, :]), axis=0
    )
    spread = jnp.sqrt(point_m2 / total_days + 1e-06)

    pair = jnp.stack([raw, other], 0)
    earlier = dslice(pair, core, 1, 0)[0]
    later = dslice(pair, 1 - core, 1, 0)[0]
    span = 2 * days_dev
    window = jnp.concatenate([earlier[:, :days_dev], later], 1).astype(jnp.float32)
    day = lax.broadcasted_iota(jnp.int32, (1, span + LMAX), 1)
    inside = (day < span) | (lax.axis_index("tz") < tz_size - 1)
    standardized = jnp.where(
        inside, (window - point_mean[:, None]) / spread[:, None], 0.0
    ).astype(jnp.bfloat16)
    out_rows = half_rows // tm_size
    own = standardized[:half_rows].reshape(tz_size, 2, out_rows, span + LMAX)
    own = dslice(own, core, 1, 1).reshape(half_rows // 2, span + LMAX)
    columns = standardized[half_rows:]

    padded = jnp.concatenate(
        [
            jnp.zeros((half_rows // 2, LMAX), jnp.bfloat16),
            own[:, :span],
            jnp.zeros((half_rows // 2, LMAX), jnp.bfloat16),
        ],
        1,
    )
    right = jnp.concatenate([columns, columns[:, :span]], 1)
    pieces = []
    for lag_index in range(NLAG):
        lag_days = lag_set[lag_index]
        left = jnp.concatenate(
            [
                dslice(padded, LMAX - lag_days, span + LMAX, 1),
                dslice(own, lag_days, span, 1),
            ],
            1,
        )
        pieces.append(
            lax.dot_general(
                left, right, (((1,), (1,)), ((), ())), preferred_element_type=jnp.float32
            )
        )
    product = jnp.concatenate(pieces, 1)

    received = lax.all_to_all(product, "tz", 0, 0, tiled=True)
    comoment = jnp.sum(received.reshape(tz_size, out_rows, -1), axis=0)
    comoment = comoment.reshape(out_rows, NLAG, K_SLOTS, block_width).transpose(0, 2, 1, 3)
    denominator = 2.0 * (total_days - lag_set).astype(jnp.float32)
    is_live = jnp.arange(K_SLOTS, dtype=jnp.int32) < live_count
    linked = jnp.where(
        is_live[None, :, None, None], comoment / denominator[None, None, :, None], 0.0
    )
    squares = jnp.sum(jnp.square(linked), axis=(1, 2, 3))
    row_scale = jnp.sqrt(squares / (live_count * NLAG * block_width).astype(jnp.float32) + 1e-06)
    return (linked / row_scale[:, None, None, None]).reshape(out_rows, -1)


def solution(mesh):
    lon_size, tm_size = mesh.devices.shape
    split = Mesh(
        mesh.devices.reshape(lon_size // 4, 4, tm_size // 2, 2), ("ly", "lx", "tz", "tc")
    )
    return jax.shard_map(
        local,
        mesh=split,
        in_specs=(P(("ly", "lx"), TIME), P(), P(), P()),
        out_specs=P(("ly", "lx") + TIME, None),
        check_vma=False,
    )
```
